256 devices in a mesh: seq: 128 (over x, y, z_lo, core), dp: 2 (over z_hi).
Axes of the slice: x: 4, y: 4, z: 8 (z_hi: 2, z_lo: 4; z = z_hi * 4 + z_lo), core: 2. Of those that a mesh axis runs over, the one named last changes fastest.
Arguments:
- inputs: bfloat16 [2, 256, 256, 512], P('dp', 'seq'), may hold values from -6 to 6
- gate: bfloat16 [2, 256, 256, 512], P('dp', 'seq'), may hold values from -6 to 6
- kernel: bfloat16 [256, 256, 512], P(None, 'seq'), may hold values from -6 to 6
- first_blocks: bfloat16 [256, 256, 256], P('seq'), may hold values from -0.375 to 0.375
- second_blocks: bfloat16 [256, 256, 256], P('seq'), may hold values from -0.375 to 0.375
- cotangent: bfloat16 [2, 256, 256, 512], P('dp', 'seq'), may hold values from -6 to 6
Outputs:
- mixed: bfloat16 [2, 256, 256, 512], P('dp', 'seq')
- grad_inputs: bfloat16 [2, 256, 256, 512], P('dp', 'seq')
- grad_gate: bfloat16 [2, 256, 256, 512], P('dp', 'seq')
- grad_kernel: float32 [256, 256, 512], P(None, 'seq')
The draws below stay inside these ranges and needn't reach their ends.
All inputs are finite; a program needn't handle non-finite values.
Results may differ from the reference program's by a relative error of at most 0.007.
Values may be sent and summed in bfloat16 or wider, within the bound.
No kernel may reach another device: no remote copies, remote signals or barrier semaphores. Data moves between devices by JAX's collectives and lax.ppermute only.
A program may use at most 64 MiB of HBM per device.

```python
import jax
import jax.numpy as jnp
from jax import lax

R = 256
C = 256
D = 512
SEQS = 2


def block_scale(rng, shape, pieces, low, top_value):
    def one(dim, blocks):
        draws = jax.random.uniform(jax.random.fold_in(jax.random.fold_in(rng, 6), dim), (blocks,), jnp.float32, low / len(pieces), top_value / len(pieces))
        return jnp.repeat(jnp.exp(draws), shape[dim] // blocks).reshape((-1,) + (1,) * (len(shape) - dim - 1))

    gain = one(*pieces[0])
    for cut in pieces[1:]:
        gain = gain * one(*cut)
    return gain


def normal_values(rng, shape, spread, reach, cuts=(), held_as=jnp.bfloat16):
    values = jax.random.normal(rng, shape, jnp.float32) * spread
    if len(cuts) > 0:
        values = block_scale(rng, shape, cuts, -0.22, 0.18) * values
    return jnp.clip(values, min=-reach, max=reach).astype(held_as)


def setup_inputs(seed: int = 0) -> dict:
    key_of = jax.random.split(jax.random.key(seed), 7)
    inputs = normal_values(key_of[0], (SEQS, R, C, D), 1.0, 6.0, ((0, 2), (1, 128)))
    gate = normal_values(key_of[1], (SEQS, R, C, D), 1.0, 6.0, ((0, 2), (1, 128)))
    kernel = normal_values(key_of[2], (R, C, D), 1.0, 6.0, ((1, 128),))
    first_blocks = normal_values(key_of[3], (R, C, C), C ** -0.5, 0.375, ((0, 128),))
    second_blocks = normal_values(key_of[4], (C, R, R), R ** -0.5, 0.375, ((0, 128),))
    cotangent = normal_values(key_of[5], (SEQS, R, C, D), 1.0, 6.0, ((0, 2), (1, 128)))
    return dict(inputs=inputs, gate=gate, kernel=kernel, first_blocks=first_blocks, second_blocks=second_blocks, cotangent=cotangent)


def one_sequence(inputs, gate, cotangent, kernel, first_blocks, second_blocks):
    f32 = jnp.float32
    bf16 = jnp.bfloat16
    kern = kernel.astype(f32)
    blk1 = first_blocks.astype(f32)
    blk2 = second_blocks.astype(f32)
    first = jnp.einsum('rij,rjd->rid', blk1, inputs.astype(f32)).astype(bf16)
    second = jnp.einsum('cqr,rcd->qcd', blk2, first.astype(f32))
    hidden = (second * kern).astype(bf16)
    third = jnp.einsum('cqr,qcd->rcd', blk2, hidden.astype(f32)).astype(bf16)
    result = jnp.einsum('rij,rid->rjd', blk1, third.astype(f32))
    gate32 = gate.astype(f32)
    mixed = (result * gate32).astype(bf16)
    cot = cotangent.astype(f32)
    d_result = (cot * gate32).astype(bf16)
    grad_gate = (cot * result).astype(bf16)
    d_third = jnp.einsum('rij,rjd->rid', blk1, d_result.astype(f32)).astype(bf16)
    d_hidden = jnp.einsum('cqr,rcd->qcd', blk2, d_third.astype(f32))
    grad_kernel = d_hidden * second
    d_second = (d_hidden * kern).astype(bf16)
    d_first = jnp.einsum('cqr,qcd->rcd', blk2, d_second.astype(f32)).astype(bf16)
    grad_inputs = jnp.einsum('rij,rid->rjd', blk1, d_first.astype(f32)).astype(bf16)
    return mixed, grad_inputs, grad_gate, grad_kernel


def reference(inputs, gate, kernel, first_blocks, second_blocks, cotangent):
    f32 = jnp.float32

    def step(carry, items):
        outs = one_sequence(items[0], items[1], items[2], kernel, first_blocks, second_blocks)
        return carry + outs[3], outs[:3]

    init = jnp.zeros((R, C, D), f32)
    total, stacked = lax.scan(step, init, (inputs, gate, cotangent))
    return stacked[0], stacked[1], stacked[2], total
```

```python
import jax
import jax.numpy as jnp
from jax import lax
from jax.sharding import PartitionSpec as P


def shards(inputs, gate, kernel, first_blocks, second_blocks, cotangent):
    f32 = jnp.float32
    bf16 = jnp.bfloat16
    seqs = inputs.shape[0]
    gate32 = gate.astype(f32)
    cot = cotangent.astype(f32)
    d_result = (cot * gate32).astype(bf16)

    def spread(rows):
        return jnp.einsum("rij,srjd->srid", first_blocks, rows, preferred_element_type=f32).astype(
            bf16
        )

    def mix_columns(piece):
        return jnp.einsum("cqr,srcd->sqcd", second_blocks, piece, preferred_element_type=f32)

    def unmix_columns(scaled):
        return jnp.einsum(
            "cqr,sqcd->srcd", second_blocks, scaled, preferred_element_type=f32
        ).astype(bf16)

    def finish_rows(piece):
        return jnp.einsum("rij,srid->srjd", first_blocks, piece, preferred_element_type=f32)

    both = jnp.concatenate([inputs, d_result], axis=0)
    mixed_both = mix_columns(
        lax.all_to_all(spread(both), "seq", split_axis=2, concat_axis=1, tiled=True)
    )
    second = mixed_both[:seqs]
    d_hidden = mixed_both[seqs:]
    partial = jnp.sum(d_hidden * second, axis=0)
    other = lax.ppermute(partial, "dp", perm=[(0, 1), (1, 0)])
    scaled = (mixed_both * kernel).astype(bf16)
    out_both = finish_rows(
        lax.all_to_all(unmix_columns(scaled), "seq", split_axis=1, concat_axis=2, tiled=True)
    )
    result = out_both[:seqs]
    d_inputs = out_both[seqs:]
    mixed = (result * gate32).astype(bf16)
    grad_gate = (cot * result).astype(bf16)
    grad_inputs = d_inputs.astype(bf16)
    grad_kernel = partial + other
    return (mixed, grad_inputs, grad_gate, grad_kernel)


def solution(mesh):
    placed = (
        P("dp", "seq", None, None),
        P("dp", "seq", None, None),
        P(None, "seq", None),
        P("seq", None, None),
        P("seq", None, None),
        P("dp", "seq", None, None),
    )
    return jax.shard_map(
        shards,
        mesh=mesh,
        in_specs=placed,
        out_specs=(
            P("dp", "seq", None, None),
            P("dp", "seq", None, None),
            P("dp", "seq", None, None),
            P(None, "seq", None),
        ),
        check_vma=False,
    )
```

```python
import jax
import jax.numpy as jnp
from jax import lax
from jax.sharding import PartitionSpec as P


def layer(inputs, gate, kernel, first_blocks, second_blocks, cotangent):
    f32 = jnp.float32
    bf16 = jnp.bfloat16
    seqs = inputs.shape[0]
    gate32 = gate.astype(f32)
    cot = cotangent.astype(f32)
    d_result = (cot * gate32).astype(bf16)

    def spread(rows):
        return jnp.einsum("rij,srjd->srid", first_blocks, rows, preferred_element_type=f32).astype(
            bf16
        )

    def mix_columns(piece):
        return jnp.einsum("cqr,srcd->sqcd", second_blocks, piece, preferred_element_type=f32)

    def unmix_columns(scaled):
        return jnp.einsum(
            "cqr,sqcd->srcd", second_blocks, scaled, preferred_element_type=f32
        ).astype(bf16)

    def finish_rows(piece):
        return jnp.einsum("rij,srid->srjd", first_blocks, piece, preferred_element_type=f32)

    both = jnp.concatenate([inputs, d_result], axis=0)
    mixed_both = mix_columns(
        lax.all_to_all(spread(both), "seq", split_axis=2, concat_axis=1, tiled=True)
    )
    second = mixed_both[:seqs]
    d_hidden = mixed_both[seqs:]
    partial = jnp.sum(d_hidden * second, axis=0)
    other = lax.ppermute(partial, "dp", perm=[(0, 1), (1, 0)])
    scaled = (mixed_both * kernel).astype(bf16)
    unmixed = unmix_columns(scaled)
    gathered = lax.all_to_all(unmixed, "seq", split_axis=1, concat_axis=2, tiled=True)
    out_both = finish_rows(gathered)
    result = out_both[:seqs]
    d_inputs = out_both[seqs:]
    mixed = (result * gate32).astype(bf16)
    grad_gate = (cot * result).astype(bf16)
    grad_inputs = d_inputs.astype(bf16)
    grad_kernel = partial + other
    return (mixed, grad_inputs, grad_gate, grad_kernel)


def solution(mesh):
    placed = (
        P("dp", "seq", None, None),
        P("dp", "seq", None, None),
        P(None, "seq", None),
        P("seq", None, None),
        P("seq", None, None),
        P("dp", "seq", None, None),
    )
    return jax.shard_map(
        layer,
        mesh=mesh,
        in_specs=placed,
        out_specs=(
            P("dp", "seq", None, None),
            P("dp", "seq", None, None),
            P("dp", "seq", None, None),
            P(None, "seq", None),
        ),
        check_vma=False,
    )
```

```python
import jax
import jax.numpy as jnp
from jax import lax
from jax.sharding import PartitionSpec as P


def layer(inputs, gate, kernel, first_blocks, second_blocks, cotangent):
    f32 = jnp.float32
    bf16 = jnp.bfloat16
    n_seq = lax.axis_size("seq")
    n_dp = lax.axis_size("dp")
    col = lax.axis_index("dp")
    cols = second_blocks.shape[0]
    rows = first_blocks.shape[0]
    width = first_blocks.shape[1]
    gate32 = gate[0].astype(f32)
    cot = cotangent[0].astype(f32)
    d_result = (cot * gate32).astype(bf16)

    blk1 = first_blocks.reshape(rows, n_seq, cols, width)
    blk1 = jnp.swapaxes(blk1, 1, 2).reshape(rows, n_seq * cols, width)
    blk2 = lax.dynamic_index_in_dim(second_blocks, col, axis=0, keepdims=False)
    kern = lax.dynamic_index_in_dim(kernel, col, axis=1, keepdims=False).astype(f32)

    both = jnp.stack([inputs[0], d_result], axis=0)
    first = jnp.einsum("rij,trjd->trid", blk1, both, preferred_element_type=f32).astype(bf16)
    cols_in = lax.all_to_all(first, ("dp", "seq"), split_axis=2, concat_axis=1, tiled=True)
    cols_in = cols_in.reshape(2, n_dp, n_seq * rows, -1)
    mixed_both = jnp.einsum("qr,tsrd->tsqd", blk2, cols_in, preferred_element_type=f32)
    second = mixed_both[0]
    d_hidden = mixed_both[1]
    own = jnp.sum(d_hidden * second, axis=0)
    other = lax.ppermute(own, "dp", perm=[(0, 1), (1, 0)])
    scaled = (mixed_both * kern).astype(bf16)
    unmixed = jnp.einsum("qr,tsqd->tsrd", blk2, scaled, preferred_element_type=f32).astype(bf16)
    unmixed = unmixed.reshape(2, n_dp, n_seq, rows, -1)
    unmixed = jnp.transpose(unmixed, (0, 3, 1, 2, 4)).reshape(2, rows, n_dp * n_seq, -1)
    gathered = lax.all_to_all(unmixed, ("dp", "seq"), split_axis=2, concat_axis=2, tiled=True)
    out_both = jnp.einsum("rij,trid->trjd", blk1, gathered, preferred_element_type=f32)
    result = out_both[0]
    mixed = (result * gate32).astype(bf16)[None]
    grad_gate = (cot * result).astype(bf16)[None]
    grad_inputs = out_both[1].astype(bf16)[None]
    pair = jnp.where(col == 0, jnp.stack([own, other], axis=1), jnp.stack([other, own], axis=1))
    return (mixed, grad_inputs, grad_gate, pair)


def solution(mesh):
    placed = (
        P("dp", "seq", None, None),
        P("dp", "seq", None, None),
        P(None, "seq", None),
        P("seq", None, None),
        P("seq", None, None),
        P("dp", "seq", None, None),
    )
    return jax.shard_map(
        layer,
        mesh=mesh,
        in_specs=placed,
        out_specs=(
            P("dp", "seq", None, None),
            P("dp", "seq", None, None),
            P("dp", "seq", None, None),
            P(None, "seq", None),
        ),
        check_vma=False,
    )
```

```python
import jax
import jax.numpy as jnp
from jax import lax
from jax.sharding import PartitionSpec as P


def layer(inputs, gate, kernel, first_blocks, second_blocks, cotangent):
    f32 = jnp.float32
    bf16 = jnp.bfloat16
    n_seq = lax.axis_size("seq")
    n_dp = lax.axis_size("dp")
    col = lax.axis_index("dp")
    cols = second_blocks.shape[0]
    rows = first_blocks.shape[0]
    width = first_blocks.shape[1]
    dm = inputs.shape[-1]
    gate32 = gate[0].astype(f32)
    cot = cotangent[0].astype(f32)
    d_result = (cot * gate32).astype(bf16)

    blk1 = first_blocks.reshape(rows, n_seq, cols, width)
    blk1 = jnp.swapaxes(blk1, 1, 2).reshape(rows, n_seq * cols, width)
    blk2 = lax.dynamic_index_in_dim(second_blocks, col, axis=0, keepdims=False)
    kern = lax.dynamic_index_in_dim(kernel, col, axis=1, keepdims=False).astype(f32)

    both = jnp.concatenate([inputs[0], d_result], axis=-1)
    first = jnp.einsum("rij,rjf->irf", blk1, both, preferred_element_type=f32).astype(bf16)
    cols_in = lax.all_to_all(first, ("dp", "seq"), split_axis=0, concat_axis=0, tiled=True)
    cols_in = cols_in.reshape(n_dp, n_seq * rows, 2 * dm)
    mixed_both = jnp.einsum("qr,srf->sqf", blk2, cols_in, preferred_element_type=f32)
    second = mixed_both[..., :dm]
    d_hidden = mixed_both[..., dm:]
    own = jnp.sum(d_hidden * second, axis=0)
    pair = lax.all_gather(own, "dp", axis=1)
    kern2 = jnp.concatenate([kern, kern], axis=-1)
    scaled = (mixed_both * kern2).astype(bf16)
    unmixed = jnp.einsum("qr,sqf->srf", blk2, scaled, preferred_element_type=f32).astype(bf16)
    unmixed = unmixed.reshape(n_dp * n_seq, rows, 2 * dm)
    gathered = lax.all_to_all(unmixed, ("dp", "seq"), split_axis=0, concat_axis=0, tiled=True)
    out_both = jnp.einsum("rij,irf->rjf", blk1, gathered, preferred_element_type=f32)
    result = out_both[..., :dm]
    mixed = (result * gate32).astype(bf16)[None]
    grad_gate = (cot * result).astype(bf16)[None]
    grad_inputs = out_both[..., dm:].astype(bf16)[None]
    return (mixed, grad_inputs, grad_gate, pair)


def solution(mesh):
    placed = (
        P("dp", "seq", None, None),
        P("dp", "seq", None, None),
        P(None, "seq", None),
        P("seq", None, None),
        P("seq", None, None),
        P("dp", "seq", None, None),
    )
    return jax.shard_map(
        layer,
        mesh=mesh,
        in_specs=placed,
        out_specs=(
            P("dp", "seq", None, None),
            P("dp", "seq", None, None),
            P("dp", "seq", None, None),
            P(None, "seq", None),
        ),
        check_vma=False,
    )
```

```python
import jax
import jax.numpy as jnp
from jax import lax
from jax.experimental.layout import Layout, with_layout_constraint
from jax.sharding import PartitionSpec as P


def layer(inputs, gate, kernel, first_blocks, second_blocks, cotangent):
    f32 = jnp.float32
    bf16 = jnp.bfloat16
    n_seq = lax.axis_size("seq")
    n_dp = lax.axis_size("dp")
    col = lax.axis_index("dp")
    cols = second_blocks.shape[0]
    rows = first_blocks.shape[0]
    width = first_blocks.shape[1]
    dm = inputs.shape[-1]
    gate32 = gate[0].astype(f32)
    cot = cotangent[0].astype(f32)
    d_result = (cot * gate32).astype(bf16)

    blk1 = first_blocks.reshape(rows, n_seq, cols, width)
    blk1 = jnp.swapaxes(blk1, 1, 2).reshape(rows, n_seq * cols, width)
    blk2 = lax.dynamic_index_in_dim(second_blocks, col, axis=0, keepdims=False)
    kern = lax.dynamic_index_in_dim(kernel, col, axis=1, keepdims=False).astype(f32)

    both = jnp.concatenate([inputs[0], d_result], axis=-1)
    first = jnp.einsum("rij,rjf->irf", first_blocks, both, preferred_element_type=f32).astype(bf16)
    cols_in = lax.all_to_all(first, ("seq", "dp"), split_axis=0, concat_axis=0, tiled=True)
    cols_in = cols_in.reshape(n_seq, n_dp, rows, 2 * dm)
    cols_in = jnp.swapaxes(cols_in, 0, 1).reshape(n_dp, n_seq * rows, 2 * dm)
    mixed_both = jnp.einsum("qr,srf->sqf", blk2, cols_in, preferred_element_type=f32)
    second = mixed_both[..., :dm]
    d_hidden = mixed_both[..., dm:]
    own = jnp.sum(d_hidden * second, axis=0)
    other = lax.ppermute(own, "dp", perm=[(0, 1), (1, 0)])
    kern2 = jnp.concatenate([kern, kern], axis=-1)
    scaled = (mixed_both * kern2).astype(bf16)
    unmixed = jnp.einsum("qr,sqf->srf", blk2, scaled, preferred_element_type=f32).astype(bf16)
    unmixed = unmixed.reshape(n_dp * n_seq, rows, 2 * dm)
    gathered = lax.all_to_all(unmixed, ("dp", "seq"), split_axis=0, concat_axis=0, tiled=True)
    out_both = jnp.einsum("rij,irf->rjf", blk1, gathered, preferred_element_type=f32)
    out_both = with_layout_constraint(out_both, Layout((0, 1, 2)))
    result = out_both[..., :dm]
    mixed = (result * gate32).astype(bf16)[None]
    grad_gate = (cot * result).astype(bf16)[None]
    grad_inputs = out_both[..., dm:].astype(bf16)[None]
    pair = jnp.where(col == 0, jnp.stack([own, other], axis=1), jnp.stack([other, own], axis=1))
    return (mixed, grad_inputs, grad_gate, pair)


def solution(mesh):
    placed = (
        P("dp", "seq", None, None),
        P("dp", "seq", None, None),
        P(None, "seq", None),
        P("seq", None, None),
        P("seq", None, None),
        P("dp", "seq", None, None),
    )
    return jax.shard_map(
        layer,
        mesh=mesh,
        in_specs=placed,
        out_specs=(
            P("dp", "seq", None, None),
            P("dp", "seq", None, None),
            P("dp", "seq", None, None),
            P(None, "seq", None),
        ),
        check_vma=False,
    )
```

```python
import jax
import jax.numpy as jnp
from jax import lax
from jax.experimental.layout import Layout, with_layout_constraint
from jax.sharding import PartitionSpec as P


def layer(inputs, gate, kernel, first_blocks, second_blocks, cotangent):
    f32 = jnp.float32
    bf16 = jnp.bfloat16
    n_seq = lax.axis_size("seq")
    n_dp = lax.axis_size("dp")
    col = lax.axis_index("dp")
    cols = second_blocks.shape[0]
    rows = first_blocks.shape[0]
    width = first_blocks.shape[1]
    dm = inputs.shape[-1]
    gate32 = gate[0].astype(f32)
    cot = cotangent[0].astype(f32)
    d_result = (cot * gate32).astype(bf16)

    blk1 = first_blocks.reshape(rows, n_seq, cols, width)
    blk1 = jnp.swapaxes(blk1, 1, 2).reshape(rows, n_seq * cols, width)
    blk2 = lax.dynamic_index_in_dim(second_blocks, col, axis=0, keepdims=False)
    kern = lax.dynamic_index_in_dim(kernel, col, axis=1, keepdims=False).astype(f32)

    both = jnp.concatenate([inputs[0], d_result], axis=-1)
    first = jnp.einsum("rij,rjf->irf", first_blocks, both, preferred_element_type=f32).astype(bf16)
    cols_in = lax.all_to_all(first, ("seq", "dp"), split_axis=0, concat_axis=0, tiled=True)
    cols_in = cols_in.reshape(n_seq, n_dp, rows, 2 * dm)
    cols_in = jnp.swapaxes(cols_in, 0, 1).reshape(n_dp, n_seq * rows, 2 * dm)
    mixed_both = jnp.einsum("qr,srf->sqf", blk2, cols_in, preferred_element_type=f32)
    second = mixed_both[..., :dm]
    d_hidden = mixed_both[..., dm:]
    own = jnp.sum(d_hidden * second, axis=0)
    other = lax.ppermute(own, "dp", perm=[(0, 1), (1, 0)])
    kern2 = jnp.concatenate([kern, kern], axis=-1)
    scaled = (mixed_both * kern2).astype(bf16)
    unmixed = jnp.einsum("qr,sqf->srf", blk2, scaled, preferred_element_type=f32).astype(bf16)
    unmixed = unmixed.reshape(n_dp * n_seq, rows, 2 * dm)
    gathered = lax.all_to_all(unmixed, ("dp", "seq"), split_axis=0, concat_axis=0, tiled=True)
    def finish(x):
        y = jnp.einsum("rij,ird->rjd", blk1, x, preferred_element_type=f32)
        return with_layout_constraint(y, Layout((0, 1, 2)))

    result = finish(gathered[..., :dm])
    mixed = (result * gate32).astype(bf16)[None]
    grad_gate = (cot * result).astype(bf16)[None]
    grad_inputs = finish(gathered[..., dm:]).astype(bf16)[None]
    pair = jnp.where(col == 0, jnp.stack([own, other], axis=1), jnp.stack([other, own], axis=1))
    return (mixed, grad_inputs, grad_gate, pair)


def solution(mesh):
    placed = (
        P("dp", "seq", None, None),
        P("dp", "seq", None, None),
        P(None, "seq", None),
        P("seq", None, None),
        P("seq", None, None),
        P("dp", "seq", None, None),
    )
    return jax.shard_map(
        layer,
        mesh=mesh,
        in_specs=placed,
        out_specs=(
            P("dp", "seq", None, None),
            P("dp", "seq", None, None),
            P("dp", "seq", None, None),
            P(None, "seq", None),
        ),
        check_vma=False,
    )
```

```python
import jax
import jax.numpy as jnp
from jax import lax
from jax.experimental.layout import Layout, with_layout_constraint
from jax.sharding import PartitionSpec as P


def layer(inputs, gate, kernel, first_blocks, second_blocks, cotangent):
    f32 = jnp.float32
    bf16 = jnp.bfloat16
    n_seq = lax.axis_size("seq")
    n_dp = lax.axis_size("dp")
    col = lax.axis_index("dp")
    cols = second_blocks.shape[0]
    rows = first_blocks.shape[0]
    width = first_blocks.shape[1]
    dm = inputs.shape[-1]
    gate32 = gate[0].astype(f32)
    cot = cotangent[0].astype(f32)
    d_result = (cot * gate32).astype(bf16)

    blk1 = first_blocks.reshape(rows, n_seq, cols, width)
    blk1 = jnp.swapaxes(blk1, 1, 2).reshape(rows, n_seq * cols, width)
    blk2 = lax.dynamic_index_in_dim(second_blocks, col, axis=0, keepdims=False)
    kern = lax.dynamic_index_in_dim(kernel, col, axis=1, keepdims=False).astype(f32)

    both = jnp.concatenate([inputs[0], d_result], axis=-1)
    first = jnp.einsum("rij,rjf->irf", first_blocks, both, preferred_element_type=f32).astype(bf16)
    cols_in = lax.all_to_all(first, ("seq", "dp"), split_axis=0, concat_axis=0, tiled=True)
    cols_in = cols_in.reshape(n_seq, n_dp, rows, 2 * dm)
    mixed_both = jnp.einsum(
        "qkl,kslf->sqf", blk2.reshape(-1, n_seq, rows), cols_in, preferred_element_type=f32
    )
    second = mixed_both[..., :dm]
    d_hidden = mixed_both[..., dm:]
    own = jnp.sum(d_hidden * second, axis=0)
    other = lax.ppermute(own, "dp", perm=[(0, 1), (1, 0)])
    kern2 = jnp.concatenate([kern, kern], axis=-1)
    scaled = (mixed_both * kern2).astype(bf16)
    unmixed = jnp.einsum("qr,sqf->srf", blk2, scaled, preferred_element_type=f32).astype(bf16)
    unmixed = unmixed.reshape(n_dp * n_seq, rows, 2 * dm)
    gathered = lax.all_to_all(unmixed, ("dp", "seq"), split_axis=0, concat_axis=0, tiled=True)
    out_both = jnp.einsum("rij,irf->rjf", blk1, gathered, preferred_element_type=f32)
    out_both = with_layout_constraint(out_both, Layout((0, 1, 2)))
    result = out_both[..., :dm]
    mixed = (result * gate32).astype(bf16)[None]
    grad_gate = (cot * result).astype(bf16)[None]
    grad_inputs = out_both[..., dm:].astype(bf16)[None]
    pair = jnp.where(col == 0, jnp.stack([own, other], axis=1), jnp.stack([other, own], axis=1))
    return (mixed, grad_inputs, grad_gate, pair)


def solution(mesh):
    placed = (
        P("dp", "seq", None, None),
        P("dp", "seq", None, None),
        P(None, "seq", None),
        P("seq", None, None),
        P("seq", None, None),
        P("dp", "seq", None, None),
    )
    return jax.shard_map(
        layer,
        mesh=mesh,
        in_specs=placed,
        out_specs=(
            P("dp", "seq", None, None),
            P("dp", "seq", None, None),
            P("dp", "seq", None, None),
            P(None, "seq", None),
        ),
        check_vma=False,
    )
```

```python
import jax
import jax.numpy as jnp
from jax import lax
from jax.experimental.layout import Layout, with_layout_constraint
from jax.sharding import PartitionSpec as P


def layer(inputs, gate, kernel, first_blocks, second_blocks, cotangent):
    f32 = jnp.float32
    bf16 = jnp.bfloat16
    n_seq = lax.axis_size("seq")
    n_dp = lax.axis_size("dp")
    col = lax.axis_index("dp")
    cols = second_blocks.shape[0]
    rows = first_blocks.shape[0]
    width = first_blocks.shape[1]
    dm = inputs.shape[-1]
    gate32 = gate[0].astype(f32)
    cot = cotangent[0].astype(f32)
    d_result = (cot * gate32).astype(bf16)

    blk1 = first_blocks.reshape(rows, n_seq, cols, width)
    blk1 = jnp.swapaxes(blk1, 1, 2).reshape(rows, n_seq * cols, width)
    blk2 = lax.dynamic_index_in_dim(second_blocks, col, axis=0, keepdims=False)
    kern = lax.dynamic_index_in_dim(kernel, col, axis=1, keepdims=False).astype(f32)

    both = jnp.concatenate([inputs[0], d_result], axis=-1)
    first = jnp.einsum("rij,rjf->irf", first_blocks, both, preferred_element_type=f32).astype(bf16)
    cols_in = lax.all_to_all(first, ("seq", "dp"), split_axis=0, concat_axis=0, tiled=True)
    cols_in = cols_in.reshape(n_seq, n_dp, rows, 2 * dm)
    mixed_both = jnp.einsum(
        "qkl,kslf->sqf", blk2.reshape(-1, n_seq, rows), cols_in, preferred_element_type=f32
    )
    second = mixed_both[..., :dm]
    d_hidden = mixed_both[..., dm:]
    own = jnp.sum(d_hidden * second, axis=0)
    other = lax.ppermute(own, "dp", perm=[(0, 1), (1, 0)])
    kern2 = jnp.concatenate([kern, kern], axis=-1)
    scaled = (mixed_both * kern2).astype(bf16)
    unmixed = jnp.einsum(
        "qkl,sqf->kslf", blk2.reshape(-1, n_seq, rows), scaled, preferred_element_type=f32
    ).astype(bf16)
    unmixed = unmixed.reshape(n_seq * n_dp, rows, 2 * dm)
    gathered = lax.all_to_all(unmixed, ("seq", "dp"), split_axis=0, concat_axis=0, tiled=True)
    out_both = jnp.einsum("rij,irf->rjf", first_blocks, gathered, preferred_element_type=f32)
    out_both = with_layout_constraint(out_both, Layout((0, 1, 2)))
    result = out_both[..., :dm]
    mixed = (result * gate32).astype(bf16)[None]
    grad_gate = (cot * result).astype(bf16)[None]
    grad_inputs = out_both[..., dm:].astype(bf16)[None]
    pair = jnp.where(col == 0, jnp.stack([own, other], axis=1), jnp.stack([other, own], axis=1))
    return (mixed, grad_inputs, grad_gate, pair)


def solution(mesh):
    placed = (
        P("dp", "seq", None, None),
        P("dp", "seq", None, None),
        P(None, "seq", None),
        P("seq", None, None),
        P("seq", None, None),
        P("dp", "seq", None, None),
    )
    return jax.shard_map(
        layer,
        mesh=mesh,
        in_specs=placed,
        out_specs=(
            P("dp", "seq", None, None),
            P("dp", "seq", None, None),
            P("dp", "seq", None, None),
            P(None, "seq", None),
        ),
        check_vma=False,
    )
```

```python
import jax
import jax.numpy as jnp
from jax import lax
from jax.experimental.layout import Layout, with_layout_constraint
from jax.sharding import PartitionSpec as P


def layer(inputs, gate, kernel, first_blocks, second_blocks, cotangent):
    f32 = jnp.float32
    bf16 = jnp.bfloat16
    n_seq = lax.axis_size("seq")
    n_dp = lax.axis_size("dp")
    col = lax.axis_index("dp")
    cols = second_blocks.shape[0]
    rows = first_blocks.shape[0]
    width = first_blocks.shape[1]
    dm = inputs.shape[-1]
    gate32 = gate[0].astype(f32)
    cot = cotangent[0].astype(f32)
    d_result = (cot * gate32).astype(bf16)

    blk1 = first_blocks.reshape(rows, n_seq, cols, width)
    blk1 = jnp.swapaxes(blk1, 1, 2).reshape(rows, n_seq * cols, width)
    blk2 = lax.dynamic_index_in_dim(second_blocks, col, axis=0, keepdims=False)
    kern = lax.dynamic_index_in_dim(kernel, col, axis=1, keepdims=False).astype(f32)

    both = jnp.concatenate([inputs[0], d_result], axis=-1)
    first = jnp.einsum("rij,rjf->irf", first_blocks, both, preferred_element_type=f32).astype(bf16)
    cols_in = lax.all_to_all(first, ("seq", "dp"), split_axis=0, concat_axis=0, tiled=True)
    cols_in = cols_in.reshape(n_seq, n_dp, rows, 2 * dm)
    mixed_both = jnp.einsum(
        "qkl,kslf->sqf", blk2.reshape(-1, n_seq, rows), cols_in, preferred_element_type=f32
    )
    second = mixed_both[..., :dm]
    d_hidden = mixed_both[..., dm:]
    own = jnp.sum(d_hidden * second, axis=0)
    half = own.shape[0] // 2
    other_a = lax.ppermute(own[:half], "dp", perm=[(0, 1), (1, 0)])
    other_b = lax.ppermute(own[half:], "dp", perm=[(0, 1), (1, 0)])
    other = jnp.concatenate([other_a, other_b], axis=0)
    kern2 = jnp.concatenate([kern, kern], axis=-1)
    scaled = (mixed_both * kern2).astype(bf16)
    unmixed = jnp.einsum("qr,sqf->srf", blk2, scaled, preferred_element_type=f32).astype(bf16)
    unmixed = unmixed.reshape(n_dp * n_seq, rows, 2 * dm)
    gathered = lax.all_to_all(unmixed, ("dp", "seq"), split_axis=0, concat_axis=0, tiled=True)
    out_both = jnp.einsum("rij,irf->rjf", blk1, gathered, preferred_element_type=f32)
    out_both = with_layout_constraint(out_both, Layout((0, 1, 2)))
    result = out_both[..., :dm]
    mixed = (result * gate32).astype(bf16)[None]
    grad_gate = (cot * result).astype(bf16)[None]
    grad_inputs = out_both[..., dm:].astype(bf16)[None]
    pair = jnp.where(col == 0, jnp.stack([own, other], axis=1), jnp.stack([other, own], axis=1))
    return (mixed, grad_inputs, grad_gate, pair)


def solution(mesh):
    placed = (
        P("dp", "seq", None, None),
        P("dp", "seq", None, None),
        P(None, "seq", None),
        P("seq", None, None),
        P("seq", None, None),
        P("dp", "seq", None, None),
    )
    return jax.shard_map(
        layer,
        mesh=mesh,
        in_specs=placed,
        out_specs=(
            P("dp", "seq", None, None),
            P("dp", "seq", None, None),
            P("dp", "seq", None, None),
            P(None, "seq", None),
        ),
        check_vma=False,
    )
```
